256 devices in a mesh: scen: 64 (over y, x, z_hi, core), trade: 4 (over z_lo).
Axes of the slice: x: 4, y: 4, z: 8 (z_hi: 2, z_lo: 4; z = z_hi * 4 + z_lo), core: 2. Of those that a mesh axis runs over, the one named last changes fastest.
Arguments:
- payoffs: float32 [12, 12, 12, 4, 8192], P(None, None, None, 'trade', 'scen'), may hold values from -4 to 4
- sweep_counts: int32 [4, 8192], P('trade', 'scen'), may hold values from 1 to 6
- netting_map: int32 [4, 8192], P('trade'), may hold values from 0 to 511
- type_lengths: int32 [8], replicated, may hold values from 1 to 8192, 32768 in all
- type_diffusion: float32 [8], replicated, may hold values from 0.02 to 0.15
- type_discount: float32 [8], replicated, may hold values from 0.01 to 0.12
- factors: float32 [3, 8192], P(None, 'scen'), may hold values from -1 to 1
Outputs:
- exposures: float32 [8192, 512], P('scen', 'trade')
- allocation: float32 [4, 8192], P('trade', 'scen')
The draws below stay inside these ranges and needn't reach their ends.
All inputs are finite; a program needn't handle non-finite values.
Results may differ from the reference program's by a relative error of at most 0.0055.
Values may be sent and summed in bfloat16 or wider, within the bound.
No kernel may reach another device: no remote copies, remote signals or barrier semaphores. Data moves between devices by JAX's collectives and lax.ppermute only.
A program may use at most 128 MiB of HBM per device.

```python
import math
import jax
import jax.numpy as jnp
import numpy as np
from jax import lax

GRID = 12
NETS = 512
TYPES = 8
MAX_SWEEPS = 6
TRADE_BLOCK = 8192
GROUPS = 4
TRADES = 32768
SCEN = 8192


def place_ends(drawn, key, least, largest):
    longest = drawn.shape.index(max(drawn.shape))
    spots = []
    for shift in (0, 1):
        where = [jax.random.randint(jax.random.fold_in(key, axis), (), 0, length) for axis, length in enumerate(drawn.shape)]
        where[longest] = (where[longest] + shift) % drawn.shape[longest]
        spots.append(tuple(where))
    return drawn.at[spots[0]].set(least).at[spots[1]].set(largest)


def shard_levels(key, shape, pieces, least, top_value):
    level, own = 1.0, jax.random.fold_in(key, 6)
    for dim, blocks in pieces:
        draws = jnp.exp(jax.random.uniform(jax.random.fold_in(own, dim), (blocks,), jnp.float32, least / len(pieces), top_value / len(pieces)))
        level = level * jnp.repeat(draws, shape[dim] // blocks).reshape([-1 if axis == dim else 1 for axis in range(len(shape))])
    return level


def split_up(number_of, total, bound, lean):
    portions = [(1 << 20) // math.isqrt(standing ** lean) + 1 for standing in range(2, number_of + 1)]
    spare, holding = total - bound - (number_of - 1), [1] * (number_of - 1)
    while spare > 0:
        movable = [i for i in range(number_of - 1) if holding[i] < bound]
        mass, left = sum([portions[i] for i in movable]), spare
        for i in movable:
            addition = min(bound - holding[i], max(1, left * portions[i] // mass), spare)
            holding[i] = holding[i] + addition
            spare = spare - addition
    return np.array([bound] + holding)


def ragged_sizes(own_key, amount, total, limit, lean):
    if amount == 2:
        one = jax.random.randint(own_key, (), max(1, total - limit), min(limit, total - 1) + 1)
        return jnp.stack([one, total - one])
    tallies = jnp.asarray(split_up(amount, total, limit, lean), jnp.int32)
    twos = (amount - 1) // 2
    source_of, receiver = tallies[1:1 + 2 * twos:2], tallies[2:2 + 2 * twos:2]
    margin = jnp.minimum(source_of - 1, limit - receiver)
    passed = jax.random.randint(jax.random.fold_in(own_key, 1), (twos,), 0, 1 << 20) % (margin + 1)
    tallies = tallies.at[1:1 + 2 * twos:2].set(source_of - passed).at[2:2 + 2 * twos:2].set(receiver + passed)
    return tallies[jax.random.permutation(jax.random.fold_in(own_key, 2), amount)]


def centred(key, dims, scale, bound, pieces=(), kind=jnp.bfloat16):
    gain = shard_levels(key, dims, pieces, -0.22, 0.18) if pieces else 1.0
    array = jax.random.normal(key, dims, jnp.float32) * scale * gain
    return jnp.minimum(jnp.maximum(array, -bound), bound).astype(kind)


def setup_inputs(seed: int = 0) -> dict:
    splits = jax.random.split(jax.random.key(seed), 8)
    return {
        "payoffs": centred(splits[0], (GRID, GRID, GRID, GROUPS, TRADE_BLOCK), 0.25, 4.0, ((3, 4), (4, 64)), jnp.float32),
        "sweep_counts": place_ends(jax.random.randint(splits[1], (GROUPS, TRADE_BLOCK), 1, MAX_SWEEPS + 1), jax.random.fold_in(splits[1], 1), 1, MAX_SWEEPS).astype(jnp.int32),
        "netting_map": place_ends(jax.random.randint(splits[2], (GROUPS, TRADE_BLOCK), 0, NETS), jax.random.fold_in(splits[2], 1), 0, NETS - 1).astype(jnp.int32),
        "type_lengths": ragged_sizes(splits[3], TYPES, TRADES, TRADES // 4, 2).astype(jnp.int32),
        "type_diffusion": jnp.clip(jnp.exp(jax.random.uniform(splits[4], (TYPES,), jnp.float32, math.log(0.02), math.log(0.15))), 0.02, 0.15),
        "type_discount": jnp.clip(jnp.exp(jax.random.uniform(splits[5], (TYPES,), jnp.float32, math.log(0.01), math.log(0.12))), 0.01, 0.12),
        "factors": jnp.clip(jax.random.uniform(splits[6], (3, SCEN), jnp.float32, -1.0, 1.0) * shard_levels(splits[6], (3, SCEN), ((1, 64),), -0.4, 0.0), -1.0, 1.0),
    }


def cheb_matrix():
    intervals = GRID - 1
    order_index = jnp.arange(GRID, dtype=jnp.float32)
    end_weights = jnp.where((order_index == 0) | (order_index == intervals), 0.5, 1.0).astype(jnp.float32)
    angles = jnp.pi * order_index[:, None] * order_index[None, :] / intervals
    return (2.0 / intervals) * end_weights[:, None] * end_weights[None, :] * jnp.cos(angles)


def cheb_basis(factors):
    factor_basis = []
    for column in range(3):
        point = factors[column]
        recurrence = [jnp.ones_like(point), point]
        for degree in range(2, GRID):
            recurrence.append(2.0 * point * recurrence[-1] - recurrence[-2])
        factor_basis.append(jnp.stack(recurrence[:GRID], 0))
    product = factor_basis[0][:, None, None, :] * factor_basis[1][None, :, None, :]
    product = product * factor_basis[2][None, None, :, :]
    return product.reshape(GRID * GRID * GRID, -1).astype(jnp.bfloat16)


def price(grid_values, counts, trade_index, type_lengths, type_diffusion, type_discount):
    type_ends = jnp.cumsum(type_lengths).astype(jnp.int32)
    type_ids = jnp.sum((trade_index[:, None] >= type_ends[None, :]).astype(jnp.int32), axis=1)
    type_hot = (type_ids[:, None] == jnp.arange(TYPES, dtype=jnp.int32)[None, :]).astype(jnp.float32)
    diffusion = jnp.sum(type_hot * type_diffusion[None, :], axis=1)
    discount = jnp.sum(type_hot * type_discount[None, :], axis=1)

    def smooth_step(degree, field):
        padded = jnp.pad(field, ((1, 1), (1, 1), (1, 1), (0, 0)))
        beside = padded[2:, 1:-1, 1:-1] + padded[:-2, 1:-1, 1:-1]
        beside = beside + padded[1:-1, 2:, 1:-1] + padded[1:-1, :-2, 1:-1]
        beside = beside + padded[1:-1, 1:-1, 2:] + padded[1:-1, 1:-1, :-2]
        updated = field + diffusion * (beside - 6.0 * field) - discount * field
        return jnp.where(degree < counts, updated, field)

    field = lax.fori_loop(0, MAX_SWEEPS, smooth_step, grid_values)
    matrix = cheb_matrix()
    field = jnp.einsum('ai,ijlp->ajlp', matrix, field, precision=lax.Precision.HIGHEST)
    field = jnp.einsum('bj,ajlp->ablp', matrix, field, precision=lax.Precision.HIGHEST)
    field = jnp.einsum('cl,ablp->abcp', matrix, field, precision=lax.Precision.HIGHEST)
    return field.reshape(GRID * GRID * GRID, -1).astype(jnp.bfloat16)


def reference(payoffs, sweep_counts, netting_map, type_lengths, type_diffusion, type_discount, factors):
    basis_rows = lax.optimization_barrier(cheb_basis(factors)).astype(jnp.float32)
    block_size = payoffs.shape[4]
    classes = jnp.arange(NETS, dtype=jnp.int32)

    def price_group(group_index):
        grid_values = lax.dynamic_index_in_dim(payoffs, group_index, 3, keepdims=False)
        counts = lax.dynamic_index_in_dim(sweep_counts, group_index, 0, keepdims=False)
        set_ids = lax.dynamic_index_in_dim(netting_map, group_index, 0, keepdims=False)
        trade_index = (group_index * block_size + jnp.arange(block_size, dtype=jnp.int32)).astype(jnp.int32)
        coef_group = price(grid_values, counts, trade_index, type_lengths, type_diffusion, type_discount)
        coef_group = lax.optimization_barrier(coef_group).astype(jnp.float32)
        values = jnp.dot(basis_rows.T, coef_group, precision=lax.Precision.HIGHEST)
        set_hot = (set_ids[:, None] == classes[None, :]).astype(jnp.float32)
        return jnp.dot(values, set_hot, precision=lax.Precision.HIGHEST), coef_group

    sums, coef_all = lax.map(price_group, jnp.arange(GROUPS, dtype=jnp.int32))
    totals = jnp.sum(sums, axis=0)
    exposures = jnp.maximum(totals, 0.0)
    scen_count = basis_rows.shape[1]
    weights = jnp.dot(basis_rows, exposures, precision=lax.Precision.HIGHEST) / scen_count

    def allocate(group_index):
        coef_group = lax.dynamic_index_in_dim(coef_all, group_index, 0, keepdims=False)
        set_ids = lax.dynamic_index_in_dim(netting_map, group_index, 0, keepdims=False)
        set_hot = (set_ids[:, None] == classes[None, :]).astype(jnp.float32)
        per_trade = jnp.dot(weights, set_hot.T, precision=lax.Precision.HIGHEST)
        return jnp.sum(coef_group * per_trade, axis=0)

    allocation = lax.map(allocate, jnp.arange(GROUPS, dtype=jnp.int32))
    return exposures, allocation
```

```python
import jax
import jax.numpy as jnp
from jax import lax
from jax.sharding import PartitionSpec as P

GRID = 12
NETS = 512
TYPES = 8
MAX_SWEEPS = 6


def cheb_matrix():
    intervals = GRID - 1
    order_index = jnp.arange(GRID, dtype=jnp.float32)
    end_weights = jnp.where((order_index == 0) | (order_index == intervals), 0.5, 1.0).astype(
        jnp.float32
    )
    angles = jnp.pi * order_index[:, None] * order_index[None, :] / intervals
    return 2.0 / intervals * end_weights[:, None] * end_weights[None, :] * jnp.cos(angles)


def cheb_basis(factors):
    factor_basis = []
    for column in range(3):
        point = factors[column]
        recurrence = [jnp.ones_like(point), point]
        for degree in range(2, GRID):
            recurrence.append(2.0 * point * recurrence[-1] - recurrence[-2])
        factor_basis.append(jnp.stack(recurrence[:GRID], 0))
    product = factor_basis[0][:, None, None, :] * factor_basis[1][None, :, None, :]
    product = product * factor_basis[2][None, None, :, :]
    return product.reshape(GRID * GRID * GRID, -1).astype(jnp.bfloat16)


def price(grid_values, counts, trade_index, type_lengths, type_diffusion, type_discount):
    type_ends = jnp.cumsum(type_lengths)
    type_ids = jnp.sum((trade_index[:, None] >= type_ends[None, :]).astype(jnp.int32), axis=1)
    type_hot = (type_ids[:, None] == jnp.arange(TYPES, dtype=jnp.int32)[None, :]).astype(
        jnp.float32
    )
    diffusion = jnp.sum(type_hot * type_diffusion[None, :], axis=1)
    discount = jnp.sum(type_hot * type_discount[None, :], axis=1)

    def smooth_step(degree, field):
        padded = jnp.pad(field, ((1, 1), (1, 1), (1, 1), (0, 0)))
        beside = padded[2:, 1:-1, 1:-1] + padded[:-2, 1:-1, 1:-1]
        beside = beside + padded[1:-1, 2:, 1:-1] + padded[1:-1, :-2, 1:-1]
        beside = beside + padded[1:-1, 1:-1, 2:] + padded[1:-1, 1:-1, :-2]
        updated = field + diffusion * (beside - 6.0 * field) - discount * field
        return jnp.where(degree < counts, updated, field)

    field = lax.fori_loop(0, MAX_SWEEPS, smooth_step, grid_values)
    matrix = cheb_matrix()
    field = jnp.einsum("ai,ijlp->ajlp", matrix, field, precision=lax.Precision.HIGHEST)
    field = jnp.einsum("bj,ajlp->ablp", matrix, field, precision=lax.Precision.HIGHEST)
    field = jnp.einsum("cl,ablp->abcp", matrix, field, precision=lax.Precision.HIGHEST)
    return field.reshape(GRID * GRID * GRID, -1).astype(jnp.bfloat16)


def shards(
    payoffs, sweep_counts, netting_map, type_lengths, type_diffusion, type_discount, factors
):
    trades_here = payoffs.shape[4]
    scen_index = lax.axis_index("scen")
    group_index = lax.axis_index("trade")
    block_size = trades_here * lax.axis_size("scen")
    first_trade = group_index * block_size + scen_index * trades_here
    trade_index = first_trade + jnp.arange(trades_here, dtype=jnp.int32)
    coef_local = price(
        payoffs[:, :, :, 0, :],
        sweep_counts[0],
        trade_index,
        type_lengths,
        type_diffusion,
        type_discount,
    )
    own_sets = lax.dynamic_slice_in_dim(netting_map[0], scen_index * trades_here, trades_here)
    coef_rows = lax.all_gather(coef_local, "trade", axis=1, tiled=True)
    set_ids = lax.all_gather(own_sets, "trade", axis=0, tiled=True)
    sets_here = NETS // lax.axis_size("trade")
    classes = group_index * sets_here + jnp.arange(sets_here, dtype=jnp.int32)
    set_hot = (set_ids[:, None] == classes[None, :]).astype(jnp.bfloat16)
    set_part = jnp.dot(coef_rows, set_hot, preferred_element_type=jnp.float32)
    set_coef = lax.psum(set_part, "scen")
    basis_rows = cheb_basis(factors).astype(jnp.float32)
    totals = lax.dot_general(
        basis_rows,
        set_coef,
        (((0,), (0,)), ((), ())),
        precision=lax.Precision.HIGHEST,
    )
    exposures = jnp.maximum(totals, 0.0)
    scen_total = factors.shape[1] * lax.axis_size("scen")
    weight_part = jnp.dot(basis_rows, exposures, precision=lax.Precision.HIGHEST)
    weights = lax.psum(weight_part, "scen") / scen_total
    trade_weights = lax.dot_general(
        coef_rows.astype(jnp.float32),
        weights,
        (((0,), (0,)), ((), ())),
        precision=lax.Precision.HIGHEST,
    )
    alloc_terms = jnp.sum(trade_weights * set_hot.astype(jnp.float32), axis=1)
    allocation = lax.psum_scatter(alloc_terms, "trade", scatter_dimension=0, tiled=True)
    return (exposures, allocation.reshape(1, trades_here))


def solution(mesh):
    return jax.shard_map(
        shards,
        mesh=mesh,
        in_specs=(
            P(None, None, None, "trade", "scen"),
            P("trade", "scen"),
            P("trade", None),
            P(),
            P(),
            P(),
            P(None, "scen"),
        ),
        out_specs=(P("scen", "trade"), P("trade", "scen")),
        check_vma=False,
    )
```

```python
import jax
import jax.numpy as jnp
from jax import lax
from jax.sharding import Mesh, PartitionSpec as P

GRID = 12
NETS = 512
TYPES = 8
MAX_SWEEPS = 6


def cheb_matrix():
    intervals = GRID - 1
    order_index = jnp.arange(GRID, dtype=jnp.float32)
    end_weights = jnp.where((order_index == 0) | (order_index == intervals), 0.5, 1.0).astype(
        jnp.float32
    )
    angles = jnp.pi * order_index[:, None] * order_index[None, :] / intervals
    return 2.0 / intervals * end_weights[:, None] * end_weights[None, :] * jnp.cos(angles)


def cheb_basis(factors):
    factor_basis = []
    for column in range(3):
        point = factors[column]
        recurrence = [jnp.ones_like(point), point]
        for degree in range(2, GRID):
            recurrence.append(2.0 * point * recurrence[-1] - recurrence[-2])
        factor_basis.append(jnp.stack(recurrence[:GRID], 0))
    product = factor_basis[0][:, None, None, :] * factor_basis[1][None, :, None, :]
    product = product * factor_basis[2][None, None, :, :]
    return product.reshape(GRID * GRID * GRID, -1).astype(jnp.bfloat16)


def price(grid_values, counts, trade_index, type_lengths, type_diffusion, type_discount):
    type_ends = jnp.cumsum(type_lengths)
    type_ids = jnp.sum((trade_index[:, None] >= type_ends[None, :]).astype(jnp.int32), axis=1)
    type_hot = (type_ids[:, None] == jnp.arange(TYPES, dtype=jnp.int32)[None, :]).astype(
        jnp.float32
    )
    diffusion = jnp.sum(type_hot * type_diffusion[None, :], axis=1)
    discount = jnp.sum(type_hot * type_discount[None, :], axis=1)

    def smooth_step(degree, field):
        padded = jnp.pad(field, ((1, 1), (1, 1), (1, 1), (0, 0)))
        beside = padded[2:, 1:-1, 1:-1] + padded[:-2, 1:-1, 1:-1]
        beside = beside + padded[1:-1, 2:, 1:-1] + padded[1:-1, :-2, 1:-1]
        beside = beside + padded[1:-1, 1:-1, 2:] + padded[1:-1, 1:-1, :-2]
        updated = field + diffusion * (beside - 6.0 * field) - discount * field
        return jnp.where(degree < counts, updated, field)

    field = lax.fori_loop(0, MAX_SWEEPS, smooth_step, grid_values)
    matrix = cheb_matrix()
    field = jnp.einsum("ai,ijlp->ajlp", matrix, field, precision=lax.Precision.HIGHEST)
    field = jnp.einsum("bj,ajlp->ablp", matrix, field, precision=lax.Precision.HIGHEST)
    field = jnp.einsum("cl,ablp->abcp", matrix, field, precision=lax.Precision.HIGHEST)
    return field.reshape(GRID * GRID * GRID, -1).astype(jnp.bfloat16)


SCEN_PARTS = (("y", 4), ("x", 4), ("zh", 2), ("core", 2))
SCEN = tuple(name for name, _ in SCEN_PARTS)


def scen_sum(part):
    for name in reversed(SCEN):
        part = lax.psum_scatter(part, name, scatter_dimension=0, tiled=True)
    for name in SCEN:
        part = lax.all_gather(part, name, axis=0, tiled=True)
    return part


def shards(
    payoffs, sweep_counts, netting_map, type_lengths, type_diffusion, type_discount, factors
):
    trades_here = payoffs.shape[4]
    scen_index = lax.axis_index(SCEN)
    group_index = lax.axis_index("trade")
    block_size = trades_here * lax.axis_size(SCEN)
    first_trade = group_index * block_size + scen_index * trades_here
    trade_index = first_trade + jnp.arange(trades_here, dtype=jnp.int32)
    coef_local = price(
        payoffs[:, :, :, 0, :],
        sweep_counts[0],
        trade_index,
        type_lengths,
        type_diffusion,
        type_discount,
    )
    own_sets = lax.dynamic_slice_in_dim(netting_map[0], scen_index * trades_here, trades_here)
    coef_rows = lax.all_gather(coef_local, "trade", axis=1, tiled=True)
    set_ids = lax.all_gather(own_sets, "trade", axis=0, tiled=True)
    sets_here = NETS // lax.axis_size("trade")
    classes = group_index * sets_here + jnp.arange(sets_here, dtype=jnp.int32)
    set_hot = (set_ids[:, None] == classes[None, :]).astype(jnp.bfloat16)
    set_part = jnp.dot(coef_rows, set_hot, preferred_element_type=jnp.float32)
    set_coef = scen_sum(set_part)
    basis_rows = cheb_basis(factors).astype(jnp.float32)
    totals = lax.dot_general(
        basis_rows,
        set_coef,
        (((0,), (0,)), ((), ())),
        precision=lax.Precision.HIGHEST,
    )
    exposures = jnp.maximum(totals, 0.0)
    scen_total = factors.shape[1] * lax.axis_size(SCEN)
    weight_part = jnp.dot(basis_rows, exposures, precision=lax.Precision.HIGHEST)
    weights = scen_sum(weight_part) / scen_total
    trade_weights = lax.dot_general(
        coef_rows.astype(jnp.float32),
        weights,
        (((0,), (0,)), ((), ())),
        precision=lax.Precision.HIGHEST,
    )
    alloc_terms = jnp.sum(trade_weights * set_hot.astype(jnp.float32), axis=1)
    allocation = lax.psum_scatter(alloc_terms, "trade", scatter_dimension=0, tiled=True)
    return (exposures, allocation.reshape(1, trades_here))


def solution(mesh):
    parts = mesh.devices.reshape(tuple(size for _, size in SCEN_PARTS) + (mesh.shape["trade"],))
    fine = Mesh(parts, SCEN + ("trade",))
    return jax.shard_map(
        shards,
        mesh=fine,
        in_specs=(
            P(None, None, None, "trade", SCEN),
            P("trade", SCEN),
            P("trade", None),
            P(),
            P(),
            P(),
            P(None, SCEN),
        ),
        out_specs=(P(SCEN, "trade"), P("trade", SCEN)),
        check_vma=False,
    )
```

```python
import jax
import jax.numpy as jnp
from jax import lax
from jax.sharding import Mesh, PartitionSpec as P

GRID = 12
NETS = 512
TYPES = 8
MAX_SWEEPS = 6


def cheb_matrix():
    intervals = GRID - 1
    order_index = jnp.arange(GRID, dtype=jnp.float32)
    end_weights = jnp.where((order_index == 0) | (order_index == intervals), 0.5, 1.0).astype(
        jnp.float32
    )
    angles = jnp.pi * order_index[:, None] * order_index[None, :] / intervals
    return 2.0 / intervals * end_weights[:, None] * end_weights[None, :] * jnp.cos(angles)


def cheb_basis(factors):
    factor_basis = []
    for column in range(3):
        point = factors[column]
        recurrence = [jnp.ones_like(point), point]
        for degree in range(2, GRID):
            recurrence.append(2.0 * point * recurrence[-1] - recurrence[-2])
        factor_basis.append(jnp.stack(recurrence[:GRID], 0))
    product = factor_basis[0][:, None, None, :] * factor_basis[1][None, :, None, :]
    product = product * factor_basis[2][None, None, :, :]
    return product.reshape(GRID * GRID * GRID, -1).astype(jnp.bfloat16)


def price(grid_values, counts, trade_index, type_lengths, type_diffusion, type_discount):
    type_ends = jnp.cumsum(type_lengths)
    type_ids = jnp.sum((trade_index[:, None] >= type_ends[None, :]).astype(jnp.int32), axis=1)
    type_hot = (type_ids[:, None] == jnp.arange(TYPES, dtype=jnp.int32)[None, :]).astype(
        jnp.float32
    )
    diffusion = jnp.sum(type_hot * type_diffusion[None, :], axis=1)
    discount = jnp.sum(type_hot * type_discount[None, :], axis=1)

    def smooth_step(degree, field):
        padded = jnp.pad(field, ((1, 1), (1, 1), (1, 1), (0, 0)))
        beside = padded[2:, 1:-1, 1:-1] + padded[:-2, 1:-1, 1:-1]
        beside = beside + padded[1:-1, 2:, 1:-1] + padded[1:-1, :-2, 1:-1]
        beside = beside + padded[1:-1, 1:-1, 2:] + padded[1:-1, 1:-1, :-2]
        updated = field + diffusion * (beside - 6.0 * field) - discount * field
        return jnp.where(degree < counts, updated, field)

    field = lax.fori_loop(0, MAX_SWEEPS, smooth_step, grid_values)
    matrix = cheb_matrix()
    field = jnp.einsum("ai,ijlp->ajlp", matrix, field, precision=lax.Precision.HIGHEST)
    field = jnp.einsum("bj,ajlp->ablp", matrix, field, precision=lax.Precision.HIGHEST)
    field = jnp.einsum("cl,ablp->abcp", matrix, field, precision=lax.Precision.HIGHEST)
    return field.reshape(GRID * GRID * GRID, -1).astype(jnp.bfloat16)


SCEN_PARTS = (("y", 4), ("x", 4), ("zh", 2), ("core", 2))
SCEN = tuple(name for name, _ in SCEN_PARTS)
SIZES = dict(SCEN_PARTS)
REDUCE_ORDER = ("core", "x", "y", "zh")


def shifted(value, name, count, shift):
    return lax.ppermute(value, name, [(j, (j + shift) % count) for j in range(count)])


def axis_scatter_sum(part, name):
    count = SIZES[name]
    own = lax.axis_index(name)
    blocks = part.reshape((count, part.shape[0] // count) + part.shape[1:])
    total = lax.dynamic_index_in_dim(blocks, own, 0, keepdims=False)
    for shift in range(1, count):
        sent = lax.dynamic_index_in_dim(blocks, (own + shift) % count, 0, keepdims=False)
        total = total + shifted(sent, name, count, shift)
    return total


def axis_gather(block, name):
    count = SIZES[name]
    own = lax.axis_index(name)
    rows = block.shape[0]
    whole = jnp.zeros((count * rows,) + block.shape[1:], block.dtype)
    whole = lax.dynamic_update_slice_in_dim(whole, block, own * rows, 0)
    for shift in range(1, count):
        got = shifted(block, name, count, shift)
        whole = lax.dynamic_update_slice_in_dim(whole, got, ((own - shift) % count) * rows, 0)
    return whole


def scen_sum(part):
    for name in REDUCE_ORDER:
        part = axis_scatter_sum(part, name)
    for name in reversed(REDUCE_ORDER):
        part = axis_gather(part, name)
    return part


def shards(
    payoffs, sweep_counts, netting_map, type_lengths, type_diffusion, type_discount, factors
):
    trades_here = payoffs.shape[4]
    scen_index = lax.axis_index(SCEN)
    group_index = lax.axis_index("trade")
    block_size = trades_here * lax.axis_size(SCEN)
    first_trade = group_index * block_size + scen_index * trades_here
    trade_index = first_trade + jnp.arange(trades_here, dtype=jnp.int32)
    coef_local = price(
        payoffs[:, :, :, 0, :],
        sweep_counts[0],
        trade_index,
        type_lengths,
        type_diffusion,
        type_discount,
    )
    own_sets = lax.dynamic_slice_in_dim(netting_map[0], scen_index * trades_here, trades_here)
    groups = lax.axis_size("trade")
    coef_rows = jnp.concatenate(
        [coef_local] + [shifted(coef_local, "trade", groups, d) for d in range(1, groups)], axis=1
    )
    set_ids = jnp.concatenate(
        [own_sets] + [shifted(own_sets, "trade", groups, d) for d in range(1, groups)], axis=0
    )
    sets_here = NETS // lax.axis_size("trade")
    classes = group_index * sets_here + jnp.arange(sets_here, dtype=jnp.int32)
    set_hot = (set_ids[:, None] == classes[None, :]).astype(jnp.bfloat16)
    set_part = jnp.dot(coef_rows, set_hot, preferred_element_type=jnp.float32)
    set_coef = scen_sum(set_part)
    basis_rows = cheb_basis(factors).astype(jnp.float32)
    totals = lax.dot_general(
        basis_rows,
        set_coef,
        (((0,), (0,)), ((), ())),
        precision=lax.Precision.HIGHEST,
    )
    exposures = jnp.maximum(totals, 0.0)
    scen_total = factors.shape[1] * lax.axis_size(SCEN)
    weight_part = jnp.dot(basis_rows, exposures, precision=lax.Precision.HIGHEST)
    weights = scen_sum(weight_part) / scen_total
    trade_weights = lax.dot_general(
        coef_rows.astype(jnp.float32),
        weights,
        (((0,), (0,)), ((), ())),
        precision=lax.Precision.HIGHEST,
    )
    alloc_terms = jnp.sum(trade_weights * set_hot.astype(jnp.float32), axis=1)
    alloc_terms = alloc_terms.reshape(groups, trades_here)
    allocation = alloc_terms[0]
    for d in range(1, groups):
        allocation = allocation + shifted(alloc_terms[d], "trade", groups, -d)
    return (exposures, allocation.reshape(1, trades_here))


def solution(mesh):
    parts = mesh.devices.reshape(tuple(size for _, size in SCEN_PARTS) + (mesh.shape["trade"],))
    fine = Mesh(parts, SCEN + ("trade",))
    return jax.shard_map(
        shards,
        mesh=fine,
        in_specs=(
            P(None, None, None, "trade", SCEN),
            P("trade", SCEN),
            P("trade", None),
            P(),
            P(),
            P(),
            P(None, SCEN),
        ),
        out_specs=(P(SCEN, "trade"), P("trade", SCEN)),
        check_vma=False,
    )
```

```python
import jax
import jax.numpy as jnp
from jax import lax
from jax.sharding import Mesh, PartitionSpec as P

GRID = 12
NETS = 512
TYPES = 8
MAX_SWEEPS = 6


def cheb_matrix():
    intervals = GRID - 1
    order_index = jnp.arange(GRID, dtype=jnp.float32)
    end_weights = jnp.where((order_index == 0) | (order_index == intervals), 0.5, 1.0).astype(
        jnp.float32
    )
    angles = jnp.pi * order_index[:, None] * order_index[None, :] / intervals
    return 2.0 / intervals * end_weights[:, None] * end_weights[None, :] * jnp.cos(angles)


def cheb_basis(factors):
    factor_basis = []
    for column in range(3):
        point = factors[column]
        recurrence = [jnp.ones_like(point), point]
        for degree in range(2, GRID):
            recurrence.append(2.0 * point * recurrence[-1] - recurrence[-2])
        factor_basis.append(jnp.stack(recurrence[:GRID], 0))
    product = factor_basis[0][:, None, None, :] * factor_basis[1][None, :, None, :]
    product = product * factor_basis[2][None, None, :, :]
    return product.reshape(GRID * GRID * GRID, -1).astype(jnp.bfloat16)


def price(grid_values, counts, trade_index, type_lengths, type_diffusion, type_discount):
    type_ends = jnp.cumsum(type_lengths)
    type_ids = jnp.sum((trade_index[:, None] >= type_ends[None, :]).astype(jnp.int32), axis=1)
    type_hot = (type_ids[:, None] == jnp.arange(TYPES, dtype=jnp.int32)[None, :]).astype(
        jnp.float32
    )
    diffusion = jnp.sum(type_hot * type_diffusion[None, :], axis=1)
    discount = jnp.sum(type_hot * type_discount[None, :], axis=1)

    def smooth_step(degree, field):
        padded = jnp.pad(field, ((1, 1), (1, 1), (1, 1), (0, 0)))
        beside = padded[2:, 1:-1, 1:-1] + padded[:-2, 1:-1, 1:-1]
        beside = beside + padded[1:-1, 2:, 1:-1] + padded[1:-1, :-2, 1:-1]
        beside = beside + padded[1:-1, 1:-1, 2:] + padded[1:-1, 1:-1, :-2]
        updated = field + diffusion * (beside - 6.0 * field) - discount * field
        return jnp.where(degree < counts, updated, field)

    field = lax.fori_loop(0, MAX_SWEEPS, smooth_step, grid_values)
    matrix = cheb_matrix()
    field = jnp.einsum("ai,ijlp->ajlp", matrix, field, precision=lax.Precision.HIGHEST)
    field = jnp.einsum("bj,ajlp->ablp", matrix, field, precision=lax.Precision.HIGHEST)
    field = jnp.einsum("cl,ablp->abcp", matrix, field, precision=lax.Precision.HIGHEST)
    return field.reshape(GRID * GRID * GRID, -1).astype(jnp.bfloat16)


SCEN_PARTS = (("y", 4), ("x", 4), ("zh", 2), ("core", 2))
SCEN = tuple(name for name, _ in SCEN_PARTS)
SIZES = dict(SCEN_PARTS)
REDUCE_ORDER = ("core", "x", "y", "zh")


def shifted(value, name, count, shift):
    return lax.ppermute(value, name, [(j, (j + shift) % count) for j in range(count)])


def axis_scatter_sum(part, name):
    count = SIZES[name]
    own = lax.axis_index(name)
    blocks = part.reshape((count, part.shape[0] // count) + part.shape[1:])
    total = lax.dynamic_index_in_dim(blocks, own, 0, keepdims=False)
    for shift in range(1, count):
        sent = lax.dynamic_index_in_dim(blocks, (own + shift) % count, 0, keepdims=False)
        total = total + shifted(sent, name, count, shift)
    return total


def axis_gather(block, name):
    count = SIZES[name]
    own = lax.axis_index(name)
    rows = block.shape[0]
    whole = jnp.zeros((count * rows,) + block.shape[1:], block.dtype)
    whole = lax.dynamic_update_slice_in_dim(whole, block, own * rows, 0)
    for shift in range(1, count):
        got = shifted(block, name, count, shift)
        whole = lax.dynamic_update_slice_in_dim(whole, got, ((own - shift) % count) * rows, 0)
    return whole


def scen_sum(part):
    for name in REDUCE_ORDER:
        part = axis_scatter_sum(part, name)
    for name in reversed(REDUCE_ORDER):
        part = axis_gather(part, name)
    return part


def shards(
    payoffs, sweep_counts, netting_map, type_lengths, type_diffusion, type_discount, factors
):
    trades_here = payoffs.shape[4]
    scen_index = lax.axis_index(SCEN)
    group_index = lax.axis_index("trade")
    block_size = trades_here * lax.axis_size(SCEN)
    first_trade = group_index * block_size + scen_index * trades_here
    trade_index = first_trade + jnp.arange(trades_here, dtype=jnp.int32)
    coef_local = price(
        payoffs[:, :, :, 0, :],
        sweep_counts[0],
        trade_index,
        type_lengths,
        type_diffusion,
        type_discount,
    )
    own_sets = lax.dynamic_slice_in_dim(netting_map[0], scen_index * trades_here, trades_here)
    rows = coef_local.shape[0]
    sent = jnp.concatenate(
        [
            coef_local,
            (own_sets // 32).astype(jnp.bfloat16)[None],
            (own_sets % 32).astype(jnp.bfloat16)[None],
            jnp.zeros((6, trades_here), jnp.bfloat16),
        ],
        axis=0,
    )
    groups = lax.axis_size("trade")
    got = jnp.concatenate(
        [sent] + [shifted(sent, "trade", groups, d) for d in range(1, groups)], axis=1
    )
    coef_rows = got[:rows]
    set_ids = got[rows].astype(jnp.int32) * 32 + got[rows + 1].astype(jnp.int32)
    sets_here = NETS // lax.axis_size("trade")
    classes = group_index * sets_here + jnp.arange(sets_here, dtype=jnp.int32)
    set_hot = (set_ids[:, None] == classes[None, :]).astype(jnp.bfloat16)
    set_part = jnp.dot(coef_rows, set_hot, preferred_element_type=jnp.float32)
    set_coef = scen_sum(set_part)
    basis_rows = cheb_basis(factors).astype(jnp.float32)
    totals = lax.dot_general(
        basis_rows,
        set_coef,
        (((0,), (0,)), ((), ())),
        precision=lax.Precision.HIGHEST,
    )
    exposures = jnp.maximum(totals, 0.0)
    scen_total = factors.shape[1] * lax.axis_size(SCEN)
    weight_part = jnp.dot(basis_rows, exposures, precision=lax.Precision.HIGHEST)
    weights = scen_sum(weight_part) / scen_total
    trade_weights = lax.dot_general(
        coef_rows.astype(jnp.float32),
        weights,
        (((0,), (0,)), ((), ())),
        precision=lax.Precision.HIGHEST,
    )
    alloc_terms = jnp.sum(trade_weights * set_hot.astype(jnp.float32), axis=1)
    alloc_terms = alloc_terms.reshape(groups, trades_here)
    allocation = alloc_terms[0]
    for d in range(1, groups):
        allocation = allocation + shifted(alloc_terms[d], "trade", groups, -d)
    return (exposures, allocation.reshape(1, trades_here))


def solution(mesh):
    parts = mesh.devices.reshape(tuple(size for _, size in SCEN_PARTS) + (mesh.shape["trade"],))
    fine = Mesh(parts, SCEN + ("trade",))
    return jax.shard_map(
        shards,
        mesh=fine,
        in_specs=(
            P(None, None, None, "trade", SCEN),
            P("trade", SCEN),
            P("trade", None),
            P(),
            P(),
            P(),
            P(None, SCEN),
        ),
        out_specs=(P(SCEN, "trade"), P("trade", SCEN)),
        check_vma=False,
    )
```

```python
import jax
import jax.numpy as jnp
from jax import lax
from jax.sharding import Mesh, PartitionSpec as P

GRID = 12
NETS = 512
TYPES = 8
MAX_SWEEPS = 6


def cheb_matrix():
    intervals = GRID - 1
    order_index = jnp.arange(GRID, dtype=jnp.float32)
    end_weights = jnp.where((order_index == 0) | (order_index == intervals), 0.5, 1.0).astype(
        jnp.float32
    )
    angles = jnp.pi * order_index[:, None] * order_index[None, :] / intervals
    return 2.0 / intervals * end_weights[:, None] * end_weights[None, :] * jnp.cos(angles)


def cheb_basis(factors):
    factor_basis = []
    for column in range(3):
        point = factors[column]
        recurrence = [jnp.ones_like(point), point]
        for degree in range(2, GRID):
            recurrence.append(2.0 * point * recurrence[-1] - recurrence[-2])
        factor_basis.append(jnp.stack(recurrence[:GRID], 0))
    product = factor_basis[0][:, None, None, :] * factor_basis[1][None, :, None, :]
    product = product * factor_basis[2][None, None, :, :]
    return product.reshape(GRID * GRID * GRID, -1).astype(jnp.bfloat16)


def price(grid_values, counts, trade_index, type_lengths, type_diffusion, type_discount):
    type_ends = jnp.cumsum(type_lengths)
    type_ids = jnp.sum((trade_index[:, None] >= type_ends[None, :]).astype(jnp.int32), axis=1)
    type_hot = (type_ids[:, None] == jnp.arange(TYPES, dtype=jnp.int32)[None, :]).astype(
        jnp.float32
    )
    diffusion = jnp.sum(type_hot * type_diffusion[None, :], axis=1)
    discount = jnp.sum(type_hot * type_discount[None, :], axis=1)

    def smooth_step(degree, field):
        padded = jnp.pad(field, ((1, 1), (1, 1), (1, 1), (0, 0)))
        beside = padded[2:, 1:-1, 1:-1] + padded[:-2, 1:-1, 1:-1]
        beside = beside + padded[1:-1, 2:, 1:-1] + padded[1:-1, :-2, 1:-1]
        beside = beside + padded[1:-1, 1:-1, 2:] + padded[1:-1, 1:-1, :-2]
        updated = field + diffusion * (beside - 6.0 * field) - discount * field
        return jnp.where(degree < counts, updated, field)

    field = lax.fori_loop(0, MAX_SWEEPS, smooth_step, grid_values)
    matrix = cheb_matrix()
    field = jnp.einsum("ai,ijlp->ajlp", matrix, field, precision=lax.Precision.HIGHEST)
    field = jnp.einsum("bj,ajlp->ablp", matrix, field, precision=lax.Precision.HIGHEST)
    field = jnp.einsum("cl,ablp->abcp", matrix, field, precision=lax.Precision.HIGHEST)
    return field.reshape(GRID * GRID * GRID, -1).astype(jnp.bfloat16)


SCEN_PARTS = (("y", 4), ("x", 4), ("zh", 2), ("core", 2))
SCEN = tuple(name for name, _ in SCEN_PARTS)
SIZES = dict(SCEN_PARTS)
def shifted(value, name, count, shift):
    return lax.ppermute(value, name, [(j, (j + shift) % count) for j in range(count)])


def axis_scatter_sum(part, name):
    count = SIZES[name]
    own = lax.axis_index(name)
    blocks = part.reshape((count, part.shape[0] // count) + part.shape[1:])
    total = lax.dynamic_index_in_dim(blocks, own, 0, keepdims=False)
    for shift in range(1, count):
        sent = lax.dynamic_index_in_dim(blocks, (own + shift) % count, 0, keepdims=False)
        total = total + shifted(sent, name, count, shift)
    return total


def axis_gather(block, name):
    count = SIZES[name]
    own = lax.axis_index(name)
    rows = block.shape[0]
    whole = jnp.zeros((count * rows,) + block.shape[1:], block.dtype)
    whole = lax.dynamic_update_slice_in_dim(whole, block, own * rows, 0)
    for shift in range(1, count):
        got = shifted(block, name, count, shift)
        whole = lax.dynamic_update_slice_in_dim(whole, got, ((own - shift) % count) * rows, 0)
    return whole


def pair_sum(part, name):
    return part + lax.ppermute(part, name, [(0, 1), (1, 0)])


def scen_sum(part):
    part = pair_sum(part, "core")
    part = axis_scatter_sum(part, "x")
    part = axis_scatter_sum(part, "y")
    part = pair_sum(part, "zh")
    part = axis_gather(part, "y")
    return axis_gather(part, "x")


def shards(
    payoffs, sweep_counts, netting_map, type_lengths, type_diffusion, type_discount, factors
):
    trades_here = payoffs.shape[4]
    scen_index = lax.axis_index(SCEN)
    group_index = lax.axis_index("trade")
    block_size = trades_here * lax.axis_size(SCEN)
    first_trade = group_index * block_size + scen_index * trades_here
    trade_index = first_trade + jnp.arange(trades_here, dtype=jnp.int32)
    coef_local = price(
        payoffs[:, :, :, 0, :],
        sweep_counts[0],
        trade_index,
        type_lengths,
        type_diffusion,
        type_discount,
    )
    own_sets = lax.dynamic_slice_in_dim(netting_map[0], scen_index * trades_here, trades_here)
    rows = coef_local.shape[0]
    sent = jnp.concatenate(
        [
            coef_local,
            (own_sets // 32).astype(jnp.bfloat16)[None],
            (own_sets % 32).astype(jnp.bfloat16)[None],
            jnp.zeros((6, trades_here), jnp.bfloat16),
        ],
        axis=0,
    )
    groups = lax.axis_size("trade")
    got = jnp.concatenate(
        [sent] + [shifted(sent, "trade", groups, d) for d in range(1, groups)], axis=1
    )
    coef_rows = got[:rows]
    set_ids = got[rows].astype(jnp.int32) * 32 + got[rows + 1].astype(jnp.int32)
    sets_here = NETS // lax.axis_size("trade")
    classes = group_index * sets_here + jnp.arange(sets_here, dtype=jnp.int32)
    set_hot = (set_ids[:, None] == classes[None, :]).astype(jnp.bfloat16)
    set_part = jnp.dot(coef_rows, set_hot, preferred_element_type=jnp.float32)
    set_coef = scen_sum(set_part)
    basis_rows = cheb_basis(factors).astype(jnp.float32)
    totals = lax.dot_general(
        basis_rows,
        set_coef,
        (((0,), (0,)), ((), ())),
        precision=lax.Precision.HIGHEST,
    )
    exposures = jnp.maximum(totals, 0.0)
    scen_total = factors.shape[1] * lax.axis_size(SCEN)
    weight_part = jnp.dot(basis_rows, exposures, precision=lax.Precision.HIGHEST)
    weights = scen_sum(weight_part) / scen_total
    trade_weights = lax.dot_general(
        coef_rows.astype(jnp.float32),
        weights,
        (((0,), (0,)), ((), ())),
        precision=lax.Precision.HIGHEST,
    )
    alloc_terms = jnp.sum(trade_weights * set_hot.astype(jnp.float32), axis=1)
    alloc_terms = alloc_terms.reshape(groups, trades_here)
    allocation = alloc_terms[0]
    for d in range(1, groups):
        allocation = allocation + shifted(alloc_terms[d], "trade", groups, -d)
    return (exposures, allocation.reshape(1, trades_here))


def solution(mesh):
    parts = mesh.devices.reshape(tuple(size for _, size in SCEN_PARTS) + (mesh.shape["trade"],))
    fine = Mesh(parts, SCEN + ("trade",))
    return jax.shard_map(
        shards,
        mesh=fine,
        in_specs=(
            P(None, None, None, "trade", SCEN),
            P("trade", SCEN),
            P("trade", None),
            P(),
            P(),
            P(),
            P(None, SCEN),
        ),
        out_specs=(P(SCEN, "trade"), P("trade", SCEN)),
        check_vma=False,
    )
```

```python
import jax
import jax.numpy as jnp
from jax import lax
from jax.sharding import Mesh, PartitionSpec as P

GRID = 12
NETS = 512
TYPES = 8
MAX_SWEEPS = 6


def cheb_matrix():
    intervals = GRID - 1
    order_index = jnp.arange(GRID, dtype=jnp.float32)
    end_weights = jnp.where((order_index == 0) | (order_index == intervals), 0.5, 1.0).astype(
        jnp.float32
    )
    angles = jnp.pi * order_index[:, None] * order_index[None, :] / intervals
    return 2.0 / intervals * end_weights[:, None] * end_weights[None, :] * jnp.cos(angles)


def cheb_basis(factors):
    factor_basis = []
    for column in range(3):
        point = factors[column]
        recurrence = [jnp.ones_like(point), point]
        for degree in range(2, GRID):
            recurrence.append(2.0 * point * recurrence[-1] - recurrence[-2])
        factor_basis.append(jnp.stack(recurrence[:GRID], 0))
    product = factor_basis[0][:, None, None, :] * factor_basis[1][None, :, None, :]
    product = product * factor_basis[2][None, None, :, :]
    return product.reshape(GRID * GRID * GRID, -1).astype(jnp.bfloat16)


def price(grid_values, counts, trade_index, type_lengths, type_diffusion, type_discount):
    type_ends = jnp.cumsum(type_lengths)
    type_ids = jnp.sum((trade_index[:, None] >= type_ends[None, :]).astype(jnp.int32), axis=1)
    type_hot = (type_ids[:, None] == jnp.arange(TYPES, dtype=jnp.int32)[None, :]).astype(
        jnp.float32
    )
    diffusion = jnp.sum(type_hot * type_diffusion[None, :], axis=1)
    discount = jnp.sum(type_hot * type_discount[None, :], axis=1)

    def smooth_step(degree, field):
        padded = jnp.pad(field, ((1, 1), (1, 1), (1, 1), (0, 0)))
        beside = padded[2:, 1:-1, 1:-1] + padded[:-2, 1:-1, 1:-1]
        beside = beside + padded[1:-1, 2:, 1:-1] + padded[1:-1, :-2, 1:-1]
        beside = beside + padded[1:-1, 1:-1, 2:] + padded[1:-1, 1:-1, :-2]
        updated = field + diffusion * (beside - 6.0 * field) - discount * field
        return jnp.where(degree < counts, updated, field)

    field = grid_values
    for degree in range(MAX_SWEEPS):
        field = smooth_step(degree, field)
    matrix = cheb_matrix()
    field = jnp.einsum("ai,ijlp->ajlp", matrix, field, precision=lax.Precision.HIGH)
    field = jnp.einsum("bj,ajlp->ablp", matrix, field, precision=lax.Precision.HIGH)
    field = jnp.einsum("cl,ablp->abcp", matrix, field, precision=lax.Precision.HIGH)
    return field.reshape(GRID * GRID * GRID, -1).astype(jnp.bfloat16)


SCEN_PARTS = (("y", 4), ("x", 4), ("zh", 2), ("core", 2))
SCEN = tuple(name for name, _ in SCEN_PARTS)
SIZES = dict(SCEN_PARTS)
def shifted(value, name, count, shift):
    return lax.ppermute(value, name, [(j, (j + shift) % count) for j in range(count)])


def axis_scatter_sum(part, name):
    count = SIZES[name]
    own = lax.axis_index(name)
    blocks = part.reshape((count, part.shape[0] // count) + part.shape[1:])
    total = lax.dynamic_index_in_dim(blocks, own, 0, keepdims=False)
    for shift in range(1, count):
        sent = lax.dynamic_index_in_dim(blocks, (own + shift) % count, 0, keepdims=False)
        total = total + shifted(sent, name, count, shift)
    return total


def axis_gather(block, name):
    count = SIZES[name]
    own = lax.axis_index(name)
    rows = block.shape[0]
    whole = jnp.zeros((count * rows,) + block.shape[1:], block.dtype)
    whole = lax.dynamic_update_slice_in_dim(whole, block, own * rows, 0)
    for shift in range(1, count):
        got = shifted(block, name, count, shift)
        whole = lax.dynamic_update_slice_in_dim(whole, got, ((own - shift) % count) * rows, 0)
    return whole


def pair_sum(part, name):
    return part + lax.ppermute(part, name, [(0, 1), (1, 0)])


def scen_sum(part):
    part = pair_sum(part, "core")
    part = axis_scatter_sum(part, "x")
    part = axis_scatter_sum(part, "y")
    part = pair_sum(part, "zh")
    part = axis_gather(part, "y")
    return axis_gather(part, "x")


def shards(
    payoffs, sweep_counts, netting_map, type_lengths, type_diffusion, type_discount, factors
):
    trades_here = payoffs.shape[4]
    scen_index = lax.axis_index(SCEN)
    group_index = lax.axis_index("trade")
    block_size = trades_here * lax.axis_size(SCEN)
    first_trade = group_index * block_size + scen_index * trades_here
    trade_index = first_trade + jnp.arange(trades_here, dtype=jnp.int32)
    coef_local = price(
        payoffs[:, :, :, 0, :],
        sweep_counts[0],
        trade_index,
        type_lengths,
        type_diffusion,
        type_discount,
    )
    own_sets = lax.dynamic_slice_in_dim(netting_map[0], scen_index * trades_here, trades_here)
    rows = coef_local.shape[0]
    sent = jnp.concatenate(
        [
            coef_local,
            (own_sets // 32).astype(jnp.bfloat16)[None],
            (own_sets % 32).astype(jnp.bfloat16)[None],
            jnp.zeros((6, trades_here), jnp.bfloat16),
        ],
        axis=0,
    )
    groups = lax.axis_size("trade")
    got = jnp.concatenate(
        [sent] + [shifted(sent, "trade", groups, d) for d in range(1, groups)], axis=1
    )
    coef_rows = got[:rows]
    set_ids = got[rows].astype(jnp.int32) * 32 + got[rows + 1].astype(jnp.int32)
    sets_here = NETS // lax.axis_size("trade")
    classes = group_index * sets_here + jnp.arange(sets_here, dtype=jnp.int32)
    set_hot = (set_ids[:, None] == classes[None, :]).astype(jnp.bfloat16)
    set_part = jnp.dot(coef_rows, set_hot, preferred_element_type=jnp.float32)
    set_coef = scen_sum(set_part)
    basis_rows = cheb_basis(factors).astype(jnp.float32)
    totals = lax.dot_general(
        basis_rows,
        set_coef,
        (((0,), (0,)), ((), ())),
        precision=lax.Precision.HIGHEST,
    )
    exposures = jnp.maximum(totals, 0.0)
    scen_total = factors.shape[1] * lax.axis_size(SCEN)
    weight_part = jnp.dot(basis_rows, exposures, precision=lax.Precision.HIGHEST)
    weights = scen_sum(weight_part) / scen_total
    trade_weights = lax.dot_general(
        coef_rows.astype(jnp.float32),
        weights,
        (((0,), (0,)), ((), ())),
        precision=lax.Precision.HIGHEST,
    )
    alloc_terms = jnp.sum(trade_weights * set_hot.astype(jnp.float32), axis=1)
    alloc_terms = alloc_terms.reshape(groups, trades_here)
    allocation = alloc_terms[0]
    for d in range(1, groups):
        allocation = allocation + shifted(alloc_terms[d], "trade", groups, -d)
    return (exposures, allocation.reshape(1, trades_here))


def solution(mesh):
    parts = mesh.devices.reshape(tuple(size for _, size in SCEN_PARTS) + (mesh.shape["trade"],))
    fine = Mesh(parts, SCEN + ("trade",))
    return jax.shard_map(
        shards,
        mesh=fine,
        in_specs=(
            P(None, None, None, "trade", SCEN),
            P("trade", SCEN),
            P("trade", None),
            P(),
            P(),
            P(),
            P(None, SCEN),
        ),
        out_specs=(P(SCEN, "trade"), P("trade", SCEN)),
        check_vma=False,
    )
```

```python
import jax
import jax.numpy as jnp
from jax import lax
from jax.sharding import Mesh, PartitionSpec as P

GRID = 12
NETS = 512
TYPES = 8
MAX_SWEEPS = 6


def cheb_matrix():
    intervals = GRID - 1
    order_index = jnp.arange(GRID, dtype=jnp.float32)
    end_weights = jnp.where((order_index == 0) | (order_index == intervals), 0.5, 1.0).astype(
        jnp.float32
    )
    angles = jnp.pi * order_index[:, None] * order_index[None, :] / intervals
    return 2.0 / intervals * end_weights[:, None] * end_weights[None, :] * jnp.cos(angles)


def cheb_basis(factors):
    factor_basis = []
    for column in range(3):
        point = factors[column]
        recurrence = [jnp.ones_like(point), point]
        for degree in range(2, GRID):
            recurrence.append(2.0 * point * recurrence[-1] - recurrence[-2])
        factor_basis.append(jnp.stack(recurrence[:GRID], 0))
    product = factor_basis[0][:, None, None, :] * factor_basis[1][None, :, None, :]
    product = product * factor_basis[2][None, None, :, :]
    return product.reshape(GRID * GRID * GRID, -1).astype(jnp.bfloat16)


def price(grid_values, counts, trade_index, type_lengths, type_diffusion, type_discount):
    type_ends = jnp.cumsum(type_lengths)
    type_ids = jnp.sum((trade_index[:, None] >= type_ends[None, :]).astype(jnp.int32), axis=1)
    type_hot = (type_ids[:, None] == jnp.arange(TYPES, dtype=jnp.int32)[None, :]).astype(
        jnp.float32
    )
    diffusion = jnp.sum(type_hot * type_diffusion[None, :], axis=1)
    discount = jnp.sum(type_hot * type_discount[None, :], axis=1)

    def smooth_step(degree, field):
        padded = jnp.pad(field, ((1, 1), (1, 1), (1, 1), (0, 0)))
        beside = padded[2:, 1:-1, 1:-1] + padded[:-2, 1:-1, 1:-1]
        beside = beside + padded[1:-1, 2:, 1:-1] + padded[1:-1, :-2, 1:-1]
        beside = beside + padded[1:-1, 1:-1, 2:] + padded[1:-1, 1:-1, :-2]
        updated = field + diffusion * (beside - 6.0 * field) - discount * field
        return jnp.where(degree < counts, updated, field)

    field = lax.fori_loop(0, MAX_SWEEPS, smooth_step, grid_values)
    matrix = cheb_matrix()
    field = jnp.einsum("ai,ijlp->ajlp", matrix, field, precision=lax.Precision.HIGH)
    field = jnp.einsum("bj,ajlp->ablp", matrix, field, precision=lax.Precision.HIGH)
    field = jnp.einsum("cl,ablp->abcp", matrix, field, precision=lax.Precision.HIGH)
    return field.reshape(GRID * GRID * GRID, -1).astype(jnp.bfloat16)


SCEN_PARTS = (("y", 4), ("x", 4), ("zh", 2), ("core", 2))
SCEN = tuple(name for name, _ in SCEN_PARTS)
SIZES = dict(SCEN_PARTS)
def shifted(value, name, count, shift):
    return lax.ppermute(value, name, [(j, (j + shift) % count) for j in range(count)])


def axis_scatter_sum(part, name):
    count = SIZES[name]
    own = lax.axis_index(name)
    blocks = part.reshape((count, part.shape[0] // count) + part.shape[1:])
    total = lax.dynamic_index_in_dim(blocks, own, 0, keepdims=False)
    for shift in range(1, count):
        sent = lax.dynamic_index_in_dim(blocks, (own + shift) % count, 0, keepdims=False)
        total = total + shifted(sent, name, count, shift)
    return total


def axis_gather(block, name):
    count = SIZES[name]
    own = lax.axis_index(name)
    rows = block.shape[0]
    whole = jnp.zeros((count * rows,) + block.shape[1:], block.dtype)
    whole = lax.dynamic_update_slice_in_dim(whole, block, own * rows, 0)
    for shift in range(1, count):
        got = shifted(block, name, count, shift)
        whole = lax.dynamic_update_slice_in_dim(whole, got, ((own - shift) % count) * rows, 0)
    return whole


def pair_sum(part, name):
    return part + lax.ppermute(part, name, [(0, 1), (1, 0)])


def scen_sum(part):
    part = axis_scatter_sum(part, "core")
    part = axis_scatter_sum(part, "x")
    part = axis_scatter_sum(part, "y")
    part = pair_sum(part, "zh")
    part = axis_gather(part, "y")
    part = axis_gather(part, "x")
    return axis_gather(part, "core")


def shards(
    payoffs, sweep_counts, netting_map, type_lengths, type_diffusion, type_discount, factors
):
    trades_here = payoffs.shape[4]
    scen_index = lax.axis_index(SCEN)
    group_index = lax.axis_index("trade")
    block_size = trades_here * lax.axis_size(SCEN)
    first_trade = group_index * block_size + scen_index * trades_here
    trade_index = first_trade + jnp.arange(trades_here, dtype=jnp.int32)
    coef_local = price(
        payoffs[:, :, :, 0, :],
        sweep_counts[0],
        trade_index,
        type_lengths,
        type_diffusion,
        type_discount,
    )
    own_sets = lax.dynamic_slice_in_dim(netting_map[0], scen_index * trades_here, trades_here)
    rows = coef_local.shape[0]
    sent = jnp.concatenate(
        [
            coef_local,
            (own_sets // 32).astype(jnp.bfloat16)[None],
            (own_sets % 32).astype(jnp.bfloat16)[None],
            jnp.zeros((6, trades_here), jnp.bfloat16),
        ],
        axis=0,
    )
    groups = lax.axis_size("trade")
    got = jnp.concatenate(
        [sent] + [shifted(sent, "trade", groups, d) for d in range(1, groups)], axis=1
    )
    coef_rows = got[:rows]
    set_ids = got[rows].astype(jnp.int32) * 32 + got[rows + 1].astype(jnp.int32)
    sets_here = NETS // lax.axis_size("trade")
    classes = group_index * sets_here + jnp.arange(sets_here, dtype=jnp.int32)
    set_hot = (set_ids[:, None] == classes[None, :]).astype(jnp.bfloat16)
    set_part = jnp.dot(coef_rows, set_hot, preferred_element_type=jnp.float32)
    set_coef = scen_sum(set_part)
    basis_rows = cheb_basis(factors).astype(jnp.float32)
    totals = lax.dot_general(
        basis_rows,
        set_coef,
        (((0,), (0,)), ((), ())),
        precision=lax.Precision.HIGHEST,
    )
    exposures = jnp.maximum(totals, 0.0)
    scen_total = factors.shape[1] * lax.axis_size(SCEN)
    weight_part = jnp.dot(basis_rows, exposures, precision=lax.Precision.HIGHEST)
    weights = scen_sum(weight_part) / scen_total
    trade_weights = lax.dot_general(
        coef_rows.astype(jnp.float32),
        weights,
        (((0,), (0,)), ((), ())),
        precision=lax.Precision.HIGHEST,
    )
    alloc_terms = jnp.sum(trade_weights * set_hot.astype(jnp.float32), axis=1)
    alloc_terms = alloc_terms.reshape(groups, trades_here)
    allocation = alloc_terms[0]
    for d in range(1, groups):
        allocation = allocation + shifted(alloc_terms[d], "trade", groups, -d)
    return (exposures, allocation.reshape(1, trades_here))


def solution(mesh):
    parts = mesh.devices.reshape(tuple(size for _, size in SCEN_PARTS) + (mesh.shape["trade"],))
    fine = Mesh(parts, SCEN + ("trade",))
    return jax.shard_map(
        shards,
        mesh=fine,
        in_specs=(
            P(None, None, None, "trade", SCEN),
            P("trade", SCEN),
            P("trade", None),
            P(),
            P(),
            P(),
            P(None, SCEN),
        ),
        out_specs=(P(SCEN, "trade"), P("trade", SCEN)),
        check_vma=False,
    )
```
